512 devices in a mesh: blk: 64 (over z, y_hi, core), grp: 8 (over x, y_lo).
Axes of the slice: x: 4, y: 8 (y_hi: 4, y_lo: 2; y = y_hi * 2 + y_lo), z: 8, core: 2. Of those that a mesh axis runs over, the one named last changes fastest.
Arguments:
- queries: bfloat16 [131072, 2048], P(('blk', 'grp')), may hold values from -100 to 100
- keys: bfloat16 [131072, 1024], P(('blk', 'grp')), may hold values from -4 to 4
- values: bfloat16 [131072, 1024], P(('blk', 'grp')), may hold values from -6 to 6
Outputs:
- attended: bfloat16 [131072, 2048], P(('blk', 'grp'))
The draws below stay inside these ranges and needn't reach their ends.
All inputs are finite; a program needn't handle non-finite values.
Results may differ from the reference program's by a relative error of at most 0.0049.
Values may be sent and summed in bfloat16 or wider, within the bound.
No kernel may reach another device: no remote copies, remote signals or barrier semaphores. Data moves between devices by JAX's collectives and lax.ppermute only.
A program may use at most 64 MiB of HBM per device.

```python
import jax
import jax.numpy as jnp
from jax import lax

HEADS = 16
KV_HEADS = 8
HEAD_DIM = 128
WINDOW = 1024
TOK_DEV = 256
TOKENS = 131072


def paired_draws(key):
    base_keys = jnp.clip(jax.random.normal(jax.random.fold_in(key, 11), (TOKENS, KV_HEADS * HEAD_DIM), jnp.float32), -3.0, 3.0)
    base_queries = jnp.clip(jax.random.normal(jax.random.fold_in(key, 12), (TOKENS, HEADS * HEAD_DIM), jnp.float32), -3.0, 3.0)
    return (base_queries, base_keys)


def draw_queries(key, part):
    return paired_draws(key)[0].astype(jnp.bfloat16)


def draw_keys(key, part):
    return paired_draws(key)[1].astype(jnp.bfloat16)


def level_of(rng, dims, cuts, smallest, top_value):
    def one(axis_at, blocks):
        draws = jax.random.uniform(jax.random.fold_in(jax.random.fold_in(rng, 6), axis_at), (blocks,), jnp.float32, smallest / len(cuts), top_value / len(cuts))
        return jnp.repeat(jnp.exp(draws), dims[axis_at] // blocks).reshape((-1,) + (1,) * (len(dims) - axis_at - 1))

    factor_of = one(*cuts[0])
    for cut in cuts[1:]:
        factor_of = factor_of * one(*cut)
    return factor_of


def gaussian(rng, extent, width, limit, split=(), kind=jnp.bfloat16):
    drawn = width * jax.random.normal(rng, extent, jnp.float32)
    if split:
        drawn = drawn * level_of(rng, extent, split, -0.22, 0.18)
    return jnp.clip(drawn, -limit, limit).astype(kind)


def setup_inputs(seed: int = 0) -> dict:
    streams_of = jax.random.split(jax.random.key(seed), 4)
    return {
        "queries": draw_queries(jax.random.fold_in(streams_of[3], 71), 0),
        "keys": draw_keys(jax.random.fold_in(streams_of[3], 71), 0),
        "values": gaussian(streams_of[2], (TOKENS, KV_HEADS * HEAD_DIM), 1.0, 6.0, ((0, 512),)),
    }


def attend_block(query_rows, key_win, value_win, block_index):
    tok_rows = query_rows.shape[0]
    group_size = HEADS // KV_HEADS
    span_rows = key_win.shape[0]
    row_ids = jnp.arange(tok_rows, dtype=jnp.int32)[:, None]
    col_ids = jnp.arange(span_rows, dtype=jnp.int32)[None, :]
    position = block_index * tok_rows - WINDOW + col_ids
    allowed = (col_ids > row_ids) & (col_ids <= row_ids + WINDOW) & (position >= 0)

    def head_group(head_index):
        query_part = lax.dynamic_slice_in_dim(query_rows, head_index * group_size * HEAD_DIM, group_size * HEAD_DIM, 1)
        query_part = query_part.reshape(tok_rows, group_size, HEAD_DIM).astype(jnp.float32)
        key_part = lax.dynamic_slice_in_dim(key_win, head_index * HEAD_DIM, HEAD_DIM, 1).astype(jnp.float32)
        value_part = lax.dynamic_slice_in_dim(value_win, head_index * HEAD_DIM, HEAD_DIM, 1).astype(jnp.float32)
        score = jnp.einsum('thd,kd->htk', query_part, key_part) * (HEAD_DIM ** -0.5)
        score = jnp.where(allowed[None], score, jnp.float32(-1e30))
        largest = jnp.max(score, axis=2, keepdims=True)
        expo = jnp.where(allowed[None], jnp.exp(score - largest), jnp.float32(0.0))
        total = jnp.sum(expo, axis=2, keepdims=True)
        weight = (expo / total).astype(jnp.bfloat16)
        output = jnp.einsum('htk,kd->thd', weight.astype(jnp.float32), value_part)
        return output.astype(jnp.bfloat16).reshape(tok_rows, group_size * HEAD_DIM)

    parts = lax.map(head_group, jnp.arange(KV_HEADS, dtype=jnp.int32))
    return jnp.transpose(parts, (1, 0, 2)).reshape(tok_rows, HEADS * HEAD_DIM)


def reference(queries, keys, values):
    padding = jnp.zeros((WINDOW, keys.shape[1]), keys.dtype)
    key_pad = jnp.concatenate([padding, keys], axis=0)
    value_pad = jnp.concatenate([padding, values], axis=0)

    def one_block(block_index):
        start_row = (block_index * TOK_DEV).astype(jnp.int32)
        query_rows = lax.dynamic_slice_in_dim(queries, start_row, TOK_DEV, 0)
        key_win = lax.dynamic_slice_in_dim(key_pad, start_row, WINDOW + TOK_DEV, 0)
        value_win = lax.dynamic_slice_in_dim(value_pad, start_row, WINDOW + TOK_DEV, 0)
        return attend_block(query_rows, key_win, value_win, block_index)

    blocks = lax.map(one_block, jnp.arange(TOKENS // TOK_DEV, dtype=jnp.int32))
    return blocks.reshape(TOKENS, HEADS * HEAD_DIM)
```

```python
import jax
import jax.numpy as jnp
from jax import lax
from jax.experimental import pallas as pl
from jax.experimental.pallas import tpu as pltpu
from jax.sharding import PartitionSpec as P

HEADS = 16
KV_HEADS = 8
HEAD_DIM = 128
WINDOW = 1024
NEG = -1e30


def from_behind(x, axis, by):
    peers = lax.axis_size(axis)
    pairs = [(i, i + by) for i in range(peers) if 0 <= i + by < peers]
    return lax.ppermute(x, axis, pairs)


def attend_kernel(valid_ref, q_ref, *refs):
    nblk = (len(refs) - 1) // 2
    k_refs, v_refs, o_ref = refs[:nblk], refs[nblk:2 * nblk], refs[-1]
    tok = q_ref.shape[0]
    row = lax.broadcasted_iota(jnp.int32, (tok, tok), 0)
    col = lax.broadcasted_iota(jnp.int32, (tok, tok), 1)
    group = HEADS // KV_HEADS
    for a in range(group):
        qa = q_ref[:, a * HEAD_DIM:(a + 1) * HEAD_DIM]
        scores = []
        for j in range(nblk):
            s = lax.dot_general(
                qa, k_refs[j][...], (((1,), (1,)), ((), ())),
                preferred_element_type=jnp.float32,
            ) * HEAD_DIM ** (-0.5)
            if j == 0:
                s = jnp.where((col > row) & (valid_ref[0] > 0), s, NEG)
            elif j == nblk - 1:
                s = jnp.where(col <= row, s, NEG)
            else:
                s = jnp.where(valid_ref[j] > 0, s, NEG)
            scores.append(s)
        largest = scores[0].max(axis=1, keepdims=True)
        for s in scores[1:]:
            largest = jnp.maximum(largest, s.max(axis=1, keepdims=True))
        expos = [jnp.exp(s - largest) for s in scores]
        total = expos[0].sum(axis=1, keepdims=True)
        for e in expos[1:]:
            total = total + e.sum(axis=1, keepdims=True)
        inv = 1.0 / total
        out = None
        for j in range(nblk):
            w = (expos[j] * inv).astype(jnp.bfloat16)
            part = jnp.dot(w, v_refs[j][...], preferred_element_type=jnp.float32)
            out = part if out is None else out + part
        o_ref[:, a * HEAD_DIM:(a + 1) * HEAD_DIM] = out.astype(o_ref.dtype)


def attend(valid, queries, k_blocks, v_blocks):
    tok = queries.shape[0]
    group = HEADS // KV_HEADS
    nblk = len(k_blocks)
    kv_spec = pl.BlockSpec((tok, HEAD_DIM), lambda h: (0, h))
    q_spec = pl.BlockSpec((tok, group * HEAD_DIM), lambda h: (0, h))
    flops = 4 * HEADS * tok * tok * nblk * HEAD_DIM
    nbytes = 2 * (2 * queries.size + 2 * nblk * k_blocks[0].size)
    return pl.pallas_call(
        attend_kernel,
        grid=(KV_HEADS,),
        in_specs=[pl.BlockSpec(memory_space=pltpu.SMEM), q_spec]
        + [kv_spec] * (2 * nblk),
        out_specs=q_spec,
        out_shape=jax.ShapeDtypeStruct(queries.shape, queries.dtype),
        cost_estimate=pl.CostEstimate(
            flops=flops, transcendentals=HEADS * tok * tok * nblk, bytes_accessed=nbytes
        ),
    )(valid, queries, *k_blocks, *v_blocks)


def body(queries, keys, values):
    tok_rows = queries.shape[0]
    back_blocks = WINDOW // tok_rows
    block_index = lax.axis_index(("blk", "grp"))
    pieces_k = []
    pieces_v = []
    for offset in range(back_blocks, 0, -1):
        moved_k, moved_v = from_behind((keys, values), ("blk", "grp"), offset)
        pieces_k.append(moved_k)
        pieces_v.append(moved_v)
    nblk = back_blocks + 1
    valid = (block_index + jnp.arange(nblk, dtype=jnp.int32) >= back_blocks).astype(jnp.int32)
    return attend(valid, queries, pieces_k + [keys], pieces_v + [values])


def solution(mesh):
    placed = (P(("blk", "grp"), None), P(("blk", "grp"), None), P(("blk", "grp"), None))
    return jax.shard_map(
        body, mesh=mesh, in_specs=placed, out_specs=P(("blk", "grp"), None), check_vma=False
    )
```

```python
import jax
import jax.numpy as jnp
from jax import lax
from jax.experimental import pallas as pl
from jax.experimental.pallas import tpu as pltpu
from jax.sharding import PartitionSpec as P

HEADS = 16
KV_HEADS = 8
HEAD_DIM = 128
WINDOW = 1024
NEG = -1e30


def from_behind(x, axis, by):
    peers = lax.axis_size(axis)
    pairs = [(i, i + by) for i in range(peers) if 0 <= i + by < peers]
    return lax.ppermute(x, axis, pairs)


def attend_kernel(valid_ref, q_ref, *refs):
    nblk = (len(refs) - 1) // 2
    k_refs, v_refs, o_ref = refs[:nblk], refs[nblk:2 * nblk], refs[-1]
    tok = q_ref.shape[0]
    row = lax.broadcasted_iota(jnp.int32, (tok, tok), 0)
    col = lax.broadcasted_iota(jnp.int32, (tok, tok), 1)
    group = HEADS // KV_HEADS
    for a in range(group):
        qa = q_ref[:, a * HEAD_DIM:(a + 1) * HEAD_DIM]
        scores = []
        for j in range(nblk):
            s = lax.dot_general(
                qa, k_refs[j][...], (((1,), (1,)), ((), ())),
                preferred_element_type=jnp.float32,
            ) * HEAD_DIM ** (-0.5)
            if j == 0:
                s = jnp.where((col > row) & (valid_ref[0] > 0), s, NEG)
            elif j == nblk - 1:
                s = jnp.where(col <= row, s, NEG)
            else:
                s = jnp.where(valid_ref[j] > 0, s, NEG)
            scores.append(s)
        largest = scores[0].max(axis=1, keepdims=True)
        for s in scores[1:]:
            largest = jnp.maximum(largest, s.max(axis=1, keepdims=True))
        expos = [jnp.exp(s - largest) for s in scores]
        total = expos[0].sum(axis=1, keepdims=True)
        for e in expos[1:]:
            total = total + e.sum(axis=1, keepdims=True)
        inv = 1.0 / total
        out = None
        for j in range(nblk):
            w = (expos[j] * inv).astype(jnp.bfloat16)
            part = jnp.dot(w, v_refs[j][...], preferred_element_type=jnp.float32)
            out = part if out is None else out + part
        o_ref[:, a * HEAD_DIM:(a + 1) * HEAD_DIM] = out.astype(o_ref.dtype)


def attend(valid, queries, k_blocks, v_blocks):
    tok = queries.shape[0]
    group = HEADS // KV_HEADS
    nblk = len(k_blocks)
    kv_spec = pl.BlockSpec((tok, HEAD_DIM), lambda h: (0, h))
    q_spec = pl.BlockSpec((tok, group * HEAD_DIM), lambda h: (0, h))
    flops = 4 * HEADS * tok * tok * nblk * HEAD_DIM
    nbytes = 2 * (2 * queries.size + 2 * nblk * k_blocks[0].size)
    return pl.pallas_call(
        attend_kernel,
        grid=(KV_HEADS,),
        in_specs=[pl.BlockSpec(memory_space=pltpu.SMEM), q_spec]
        + [kv_spec] * (2 * nblk),
        out_specs=q_spec,
        out_shape=jax.ShapeDtypeStruct(queries.shape, queries.dtype),
        cost_estimate=pl.CostEstimate(
            flops=flops, transcendentals=HEADS * tok * tok * nblk, bytes_accessed=nbytes
        ),
    )(valid, queries, *k_blocks, *v_blocks)


def shifted(x, axis, pairs):
    return lax.ppermute(x, axis, pairs)


def body(queries, keys, values):
    axis = ("blk", "grp")
    n = lax.axis_size(axis)
    block_index = lax.axis_index(axis)
    own = (keys, values)
    ahead2 = [(i, i + 2) for i in range(n) if i + 2 < n]
    x1 = shifted(own, axis, ahead2)
    y1 = shifted(own, axis, [(i, i + 1) for i in range(0, n, 2)])
    x2 = shifted(x1, axis, ahead2)
    y2 = shifted(x1, axis, [(i, i ^ 1) for i in range(n)])
    y3 = shifted(x2, axis, [(i, i - 1) for i in range(1, n, 2)])
    odd = (block_index % 2) == 1
    b1 = [jnp.where(odd, a, b) for a, b in zip(y1, y2)]
    b3 = [jnp.where(odd, a, b) for a, b in zip(y2, y3)]
    back_blocks = WINDOW // queries.shape[0]
    nblk = back_blocks + 1
    valid = (block_index + jnp.arange(nblk, dtype=jnp.int32) >= back_blocks).astype(jnp.int32)
    k_blocks = [x2[0], b3[0], x1[0], b1[0], keys]
    v_blocks = [x2[1], b3[1], x1[1], b1[1], values]
    return attend(valid, queries, k_blocks, v_blocks)


def solution(mesh):
    placed = (P(("blk", "grp"), None), P(("blk", "grp"), None), P(("blk", "grp"), None))
    return jax.shard_map(
        body, mesh=mesh, in_specs=placed, out_specs=P(("blk", "grp"), None), check_vma=False
    )
```

```python
import jax
import jax.numpy as jnp
from jax import lax
from jax.experimental import pallas as pl
from jax.experimental.pallas import tpu as pltpu
from jax.sharding import PartitionSpec as P

HEADS = 16
KV_HEADS = 8
HEAD_DIM = 128
WINDOW = 1024
NEG = -1e30


def from_behind(x, axis, by):
    peers = lax.axis_size(axis)
    pairs = [(i, i + by) for i in range(peers) if 0 <= i + by < peers]
    return lax.ppermute(x, axis, pairs)


def attend_kernel(valid_ref, q_ref, *refs):
    nblk = (len(refs) - 1) // 2
    k_refs, v_refs, o_ref = refs[:nblk], refs[nblk:2 * nblk], refs[-1]
    tok = q_ref.shape[0]
    row = lax.broadcasted_iota(jnp.int32, (tok, tok), 0)
    col = lax.broadcasted_iota(jnp.int32, (tok, tok), 1)
    group = HEADS // KV_HEADS
    for a in range(group):
        qa = q_ref[:, a * HEAD_DIM:(a + 1) * HEAD_DIM]
        scores = []
        for j in range(nblk):
            s = lax.dot_general(
                qa, k_refs[j][...], (((1,), (1,)), ((), ())),
                preferred_element_type=jnp.float32,
            ) * HEAD_DIM ** (-0.5)
            if j == 0:
                s = jnp.where((col > row) & (valid_ref[0] > 0), s, NEG)
            elif j == nblk - 1:
                s = jnp.where(col <= row, s, NEG)
            else:
                s = jnp.where(valid_ref[j] > 0, s, NEG)
            scores.append(s)
        largest = scores[0].max(axis=1, keepdims=True)
        for s in scores[1:]:
            largest = jnp.maximum(largest, s.max(axis=1, keepdims=True))
        expos = [jnp.exp(s - largest) for s in scores]
        total = expos[0].sum(axis=1, keepdims=True)
        for e in expos[1:]:
            total = total + e.sum(axis=1, keepdims=True)
        inv = 1.0 / total
        out = None
        for j in range(nblk):
            w = (expos[j] * inv).astype(jnp.bfloat16)
            part = jnp.dot(w, v_refs[j][...], preferred_element_type=jnp.float32)
            out = part if out is None else out + part
        o_ref[:, a * HEAD_DIM:(a + 1) * HEAD_DIM] = out.astype(o_ref.dtype)


def attend(valid, queries, k_blocks, v_blocks):
    tok = queries.shape[0]
    group = HEADS // KV_HEADS
    nblk = len(k_blocks)
    k_spec = pl.BlockSpec((tok, HEAD_DIM), lambda h: (0, h))
    v_spec = pl.BlockSpec((tok, HEAD_DIM), lambda h: (0, KV_HEADS + h))
    q_spec = pl.BlockSpec((tok, group * HEAD_DIM), lambda h: (0, h))
    flops = 4 * HEADS * tok * tok * nblk * HEAD_DIM
    nbytes = 2 * (2 * queries.size + nblk * k_blocks[0].size)
    return pl.pallas_call(
        attend_kernel,
        grid=(KV_HEADS,),
        in_specs=[pl.BlockSpec(memory_space=pltpu.SMEM), q_spec]
        + [k_spec] * nblk + [v_spec] * nblk,
        out_specs=q_spec,
        out_shape=jax.ShapeDtypeStruct(queries.shape, queries.dtype),
        cost_estimate=pl.CostEstimate(
            flops=flops, transcendentals=HEADS * tok * tok * nblk, bytes_accessed=nbytes
        ),
    )(valid, queries, *k_blocks, *v_blocks)


def attend_kv(valid, queries, kv_blocks):
    return attend(valid, queries, kv_blocks, kv_blocks)


def shifted(x, axis, pairs):
    return lax.ppermute(x, axis, pairs)


def body(queries, keys, values):
    axis = ("blk", "grp")
    n = lax.axis_size(axis)
    block_index = lax.axis_index(axis)
    own = jnp.concatenate([keys, values], axis=1)
    ahead2 = [(i, i + 2) for i in range(n) if i + 2 < n]
    x1 = shifted(own, axis, ahead2)
    y1 = shifted(own, axis, [(i, i + 1) for i in range(0, n, 2)])
    x2 = shifted(x1, axis, ahead2)
    y2 = shifted(x1, axis, [(i, i ^ 1) for i in range(n)])
    y3 = shifted(x2, axis, [(i, i - 1) for i in range(1, n, 2)])
    odd = (block_index % 2) == 1
    b1 = jnp.where(odd, y1, y2)
    b3 = jnp.where(odd, y2, y3)
    back_blocks = WINDOW // queries.shape[0]
    nblk = back_blocks + 1
    valid = (block_index + jnp.arange(nblk, dtype=jnp.int32) >= back_blocks).astype(jnp.int32)
    return attend_kv(valid, queries, [x2, b3, x1, b1, own])


def solution(mesh):
    placed = (P(("blk", "grp"), None), P(("blk", "grp"), None), P(("blk", "grp"), None))
    return jax.shard_map(
        body, mesh=mesh, in_specs=placed, out_specs=P(("blk", "grp"), None), check_vma=False
    )
```

```python
import functools

import jax
import jax.numpy as jnp
from jax import lax
from jax.experimental import pallas as pl
from jax.experimental.pallas import tpu as pltpu
from jax.sharding import PartitionSpec as P

HEADS = 16
KV_HEADS = 8
HEAD_DIM = 128
WINDOW = 1024
NEG = -1e30
GROUP = HEADS // KV_HEADS

LOWER, UPPER, WHOLE = 0, 1, 2


def step_kernel(kinds, first, last, valid_ref, q_ref, *refs):
    nblk = len(kinds)
    k_refs, v_refs = refs[:nblk], refs[nblk:2 * nblk]
    rest = refs[2 * nblk:]
    if not first:
        m_in, l_in, acc_in = rest[:3]
        rest = rest[3:]
    tok = q_ref.shape[0]
    h = pl.program_id(0)
    row = lax.broadcasted_iota(jnp.int32, (tok, tok), 0)
    col = lax.broadcasted_iota(jnp.int32, (tok, tok), 1)
    lane = lax.broadcasted_iota(jnp.int32, (tok, HEADS), 1)
    for a in range(GROUP):
        qa = q_ref[:, a * HEAD_DIM:(a + 1) * HEAD_DIM]
        here = lane == h * GROUP + a
        scores = []
        for j, kind in enumerate(kinds):
            s = lax.dot_general(
                qa, k_refs[j][...], (((1,), (1,)), ((), ())),
                preferred_element_type=jnp.float32,
            ) * HEAD_DIM ** (-0.5)
            keep = valid_ref[j] > 0
            if kind == LOWER:
                keep = (col <= row) & keep
            elif kind == UPPER:
                keep = (col > row) & keep
            scores.append(jnp.where(keep, s, NEG))
        largest = scores[0].max(axis=1, keepdims=True)
        for s in scores[1:]:
            largest = jnp.maximum(largest, s.max(axis=1, keepdims=True))
        if not first:
            m_old = jnp.sum(jnp.where(here, m_in[...], 0.0), axis=1, keepdims=True)
            l_old = jnp.sum(jnp.where(here, l_in[...], 0.0), axis=1, keepdims=True)
            largest = jnp.maximum(largest, m_old)
        expos = [jnp.exp(s - largest) for s in scores]
        total = expos[0].sum(axis=1, keepdims=True)
        for e in expos[1:]:
            total = total + e.sum(axis=1, keepdims=True)
        acc = None
        for j in range(nblk):
            hi = expos[j].astype(jnp.bfloat16)
            lo = (expos[j] - hi.astype(jnp.float32)).astype(jnp.bfloat16)
            vj = v_refs[j][...]
            part = jnp.dot(hi, vj, preferred_element_type=jnp.float32) + jnp.dot(
                lo, vj, preferred_element_type=jnp.float32
            )
            acc = part if acc is None else acc + part
        cols = slice(a * HEAD_DIM, (a + 1) * HEAD_DIM)
        if not first:
            scale = jnp.exp(m_old - largest)
            total = total + scale * l_old
            acc = acc + scale * acc_in[:, cols]
        if last:
            rest[0][:, cols] = (acc * (1.0 / total)).astype(rest[0].dtype)
        else:
            m_out, l_out, acc_out = rest
            acc_out[:, cols] = acc
            m_out[...] = jnp.where(here, largest, m_out[...])
            l_out[...] = jnp.where(here, total, l_out[...])


def attend_step(kinds, first, last, valid, queries, kv_blocks, state):
    tok = queries.shape[0]
    nblk = len(kinds)
    k_spec = pl.BlockSpec((tok, HEAD_DIM), lambda h: (0, h))
    v_spec = pl.BlockSpec((tok, HEAD_DIM), lambda h: (0, KV_HEADS + h))
    q_spec = pl.BlockSpec((tok, GROUP * HEAD_DIM), lambda h: (0, h))
    stat_spec = pl.BlockSpec((tok, HEADS), lambda h: (0, 0))
    in_specs = [pl.BlockSpec(memory_space=pltpu.SMEM), q_spec]
    in_specs += [k_spec] * nblk + [v_spec] * nblk
    args = [valid, queries, *kv_blocks, *kv_blocks]
    if not first:
        in_specs += [stat_spec, stat_spec, q_spec]
        args += list(state)
    if last:
        out_specs = q_spec
        out_shape = jax.ShapeDtypeStruct(queries.shape, queries.dtype)
    else:
        out_specs = [stat_spec, stat_spec, q_spec]
        out_shape = [
            jax.ShapeDtypeStruct((tok, HEADS), jnp.float32),
            jax.ShapeDtypeStruct((tok, HEADS), jnp.float32),
            jax.ShapeDtypeStruct(queries.shape, jnp.float32),
        ]
    flops = 4 * HEADS * tok * tok * nblk * HEAD_DIM
    nbytes = 2 * queries.size * (2 if last else 1) + 2 * nblk * kv_blocks[0].size
    nbytes += (0 if first else 4 * queries.size) + (0 if last else 4 * queries.size)
    return pl.pallas_call(
        functools.partial(step_kernel, tuple(kinds), first, last),
        grid=(KV_HEADS,),
        in_specs=in_specs,
        out_specs=out_specs,
        out_shape=out_shape,
        cost_estimate=pl.CostEstimate(
            flops=flops, transcendentals=HEADS * tok * tok * nblk, bytes_accessed=nbytes
        ),
    )(*args)


def shifted(x, axis, pairs):
    return lax.ppermute(x, axis, pairs)


def flags(*conds):
    return jnp.stack([c.astype(jnp.int32) for c in conds])


def body(queries, keys, values):
    axis = ("blk", "grp")
    n = lax.axis_size(axis)
    d = lax.axis_index(axis)
    odd = (d % 2) == 1
    own = jnp.concatenate([keys, values], axis=1)
    ahead2 = [(i, i + 2) for i in range(n) if i + 2 < n]
    x1 = shifted(own, axis, ahead2)
    y1 = shifted(own, axis, [(i, i + 1) for i in range(0, n, 2)])
    x1, y1 = lax.optimization_barrier((x1, y1))
    x2 = shifted(x1, axis, ahead2)
    y2 = shifted(x1, axis, [(i, i ^ 1) for i in range(n)])
    y3 = shifted(x2, axis, [(i, i - 1) for i in range(1, n, 2)])

    v1 = flags(d >= 0, d >= 2, odd)
    state = attend_step((LOWER, WHOLE, WHOLE), True, False, v1, queries, [own, x1, y1], None)
    v2 = flags(d >= 4, d >= jnp.where(odd, 3, 1))
    state = attend_step((UPPER, WHOLE), False, False, v2, queries, [x2, y2], state)
    v3 = flags(jnp.logical_not(odd) & (d >= 3))
    return attend_step((WHOLE,), False, True, v3, queries, [y3], state)


def solution(mesh):
    placed = (P(("blk", "grp"), None), P(("blk", "grp"), None), P(("blk", "grp"), None))
    return jax.shard_map(
        body, mesh=mesh, in_specs=placed, out_specs=P(("blk", "grp"), None), check_vma=False
    )
```

```python
import jax
import jax.numpy as jnp
from jax import lax
from jax.experimental import pallas as pl
from jax.experimental.pallas import tpu as pltpu
from jax.sharding import PartitionSpec as P

HEADS = 16
KV_HEADS = 8
HEAD_DIM = 128
WINDOW = 1024
NEG = -1e30


def from_behind(x, axis, by):
    peers = lax.axis_size(axis)
    pairs = [(i, i + by) for i in range(peers) if 0 <= i + by < peers]
    return lax.ppermute(x, axis, pairs)


def attend_kernel(valid_ref, q_ref, *refs):
    nblk = (len(refs) - 1) // 2
    k_refs, v_refs, o_ref = refs[:nblk], refs[nblk:2 * nblk], refs[-1]
    tok = q_ref.shape[0]
    row = lax.broadcasted_iota(jnp.int32, (tok, tok), 0)
    col = lax.broadcasted_iota(jnp.int32, (tok, tok), 1)
    group = HEADS // KV_HEADS
    for a in range(group):
        qa = q_ref[:, a * HEAD_DIM:(a + 1) * HEAD_DIM]
        scores = []
        for j in range(nblk):
            s = lax.dot_general(
                qa, k_refs[j][...], (((1,), (1,)), ((), ())),
                preferred_element_type=jnp.float32,
            ) * HEAD_DIM ** (-0.5)
            if j == 0:
                s = jnp.where((col > row) & (valid_ref[0] > 0), s, NEG)
            elif j == nblk - 1:
                s = jnp.where(col <= row, s, NEG)
            else:
                s = jnp.where(valid_ref[j] > 0, s, NEG)
            scores.append(s)
        largest = scores[0].max(axis=1, keepdims=True)
        for s in scores[1:]:
            largest = jnp.maximum(largest, s.max(axis=1, keepdims=True))
        expos = [jnp.exp(s - largest) for s in scores]
        total = expos[0].sum(axis=1, keepdims=True)
        for e in expos[1:]:
            total = total + e.sum(axis=1, keepdims=True)
        inv = 1.0 / total
        out = None
        for j in range(nblk):
            w = (expos[j] * inv).astype(jnp.bfloat16)
            part = jnp.dot(w, v_refs[j][...], preferred_element_type=jnp.float32)
            out = part if out is None else out + part
        o_ref[:, a * HEAD_DIM:(a + 1) * HEAD_DIM] = out.astype(o_ref.dtype)


def attend(valid, queries, k_blocks, v_blocks):
    tok = queries.shape[0]
    group = HEADS // KV_HEADS
    nblk = len(k_blocks)
    kv_spec = pl.BlockSpec((tok, HEAD_DIM), lambda h: (0, h))
    q_spec = pl.BlockSpec((tok, group * HEAD_DIM), lambda h: (0, h))
    flops = 4 * HEADS * tok * tok * nblk * HEAD_DIM
    nbytes = 2 * (2 * queries.size + 2 * nblk * k_blocks[0].size)
    return pl.pallas_call(
        attend_kernel,
        grid=(KV_HEADS,),
        in_specs=[pl.BlockSpec(memory_space=pltpu.SMEM), q_spec]
        + [kv_spec] * (2 * nblk),
        out_specs=q_spec,
        out_shape=jax.ShapeDtypeStruct(queries.shape, queries.dtype),
        cost_estimate=pl.CostEstimate(
            flops=flops, transcendentals=HEADS * tok * tok * nblk, bytes_accessed=nbytes
        ),
    )(valid, queries, *k_blocks, *v_blocks)


def shifted(x, axis, pairs):
    return lax.ppermute(x, axis, pairs)


def body(queries, keys, values):
    axis = ("blk", "grp")
    n = lax.axis_size(axis)
    block_index = lax.axis_index(axis)
    own = (keys, values)
    ahead2 = [(i, i + 2) for i in range(n) if i + 2 < n]
    x1 = shifted(own, axis, ahead2)
    y1 = shifted(own, axis, [(i, i + 1) for i in range(0, n, 2)])
    fenced = [lax.optimization_barrier((a, b)) for a, b in zip(x1, y1)]
    x1 = tuple(f[0] for f in fenced)
    y1 = tuple(f[1] for f in fenced)
    x2 = shifted(x1, axis, ahead2)
    y2 = shifted(x1, axis, [(i, i ^ 1) for i in range(n)])
    y3 = shifted(x2, axis, [(i, i - 1) for i in range(1, n, 2)])
    odd = (block_index % 2) == 1
    b1 = [jnp.where(odd, a, b) for a, b in zip(y1, y2)]
    b3 = [jnp.where(odd, a, b) for a, b in zip(y2, y3)]
    back_blocks = WINDOW // queries.shape[0]
    nblk = back_blocks + 1
    valid = (block_index + jnp.arange(nblk, dtype=jnp.int32) >= back_blocks).astype(jnp.int32)
    k_blocks = [x2[0], b3[0], x1[0], b1[0], keys]
    v_blocks = [x2[1], b3[1], x1[1], b1[1], values]
    return attend(valid, queries, k_blocks, v_blocks)


def solution(mesh):
    placed = (P(("blk", "grp"), None), P(("blk", "grp"), None), P(("blk", "grp"), None))
    return jax.shard_map(
        body, mesh=mesh, in_specs=placed, out_specs=P(("blk", "grp"), None), check_vma=False
    )
```

```python
import functools

import jax
import jax.numpy as jnp
from jax import lax
from jax.experimental import pallas as pl
from jax.experimental.pallas import tpu as pltpu
from jax.sharding import PartitionSpec as P

HEADS = 16
KV_HEADS = 8
HEAD_DIM = 128
WINDOW = 1024
NEG = -1e30
GROUP = HEADS // KV_HEADS

LOWER, UPPER, WHOLE = 0, 1, 2


def step_kernel(kinds, first, last, valid_ref, q_ref, *refs):
    nblk = len(kinds)
    k_refs, v_refs = refs[:nblk], refs[nblk:2 * nblk]
    rest = refs[2 * nblk:]
    if not first:
        m_in, l_in, acc_in = rest[:3]
        rest = rest[3:]
    tok = q_ref.shape[0]
    h = pl.program_id(0)
    row = lax.broadcasted_iota(jnp.int32, (tok, tok), 0)
    col = lax.broadcasted_iota(jnp.int32, (tok, tok), 1)
    lane = lax.broadcasted_iota(jnp.int32, (tok, HEADS), 1)
    for a in range(GROUP):
        qa = q_ref[:, a * HEAD_DIM:(a + 1) * HEAD_DIM]
        here = lane == h * GROUP + a
        scores = []
        for j, kind in enumerate(kinds):
            s = lax.dot_general(
                qa, k_refs[j][...], (((1,), (1,)), ((), ())),
                preferred_element_type=jnp.float32,
            ) * HEAD_DIM ** (-0.5)
            keep = valid_ref[j] > 0
            if kind == LOWER:
                keep = (col <= row) & keep
            elif kind == UPPER:
                keep = (col > row) & keep
            scores.append(jnp.where(keep, s, NEG))
        largest = scores[0].max(axis=1, keepdims=True)
        for s in scores[1:]:
            largest = jnp.maximum(largest, s.max(axis=1, keepdims=True))
        if not first:
            m_old = jnp.sum(jnp.where(here, m_in[...], 0.0), axis=1, keepdims=True)
            l_old = jnp.sum(jnp.where(here, l_in[...], 0.0), axis=1, keepdims=True)
            largest = jnp.maximum(largest, m_old)
        expos = [jnp.exp(s - largest) for s in scores]
        total = expos[0].sum(axis=1, keepdims=True)
        for e in expos[1:]:
            total = total + e.sum(axis=1, keepdims=True)
        acc = None
        for j in range(nblk):
            hi = expos[j].astype(jnp.bfloat16)
            lo = (expos[j] - hi.astype(jnp.float32)).astype(jnp.bfloat16)
            vj = v_refs[j][...]
            part = jnp.dot(hi, vj, preferred_element_type=jnp.float32) + jnp.dot(
                lo, vj, preferred_element_type=jnp.float32
            )
            acc = part if acc is None else acc + part
        cols = slice(a * HEAD_DIM, (a + 1) * HEAD_DIM)
        if not first:
            scale = jnp.exp(m_old - largest)
            total = total + scale * l_old
            acc = acc + scale * acc_in[:, cols]
        if last:
            rest[0][:, cols] = (acc * (1.0 / total)).astype(rest[0].dtype)
        else:
            m_out, l_out, acc_out = rest
            acc_out[:, cols] = acc
            m_out[...] = jnp.where(here, largest, m_out[...])
            l_out[...] = jnp.where(here, total, l_out[...])


def attend_step(kinds, first, last, valid, queries, k_blocks, v_blocks, state):
    tok = queries.shape[0]
    nblk = len(kinds)
    k_spec = pl.BlockSpec((tok, HEAD_DIM), lambda h: (0, h))
    v_spec = k_spec
    q_spec = pl.BlockSpec((tok, GROUP * HEAD_DIM), lambda h: (0, h))
    stat_spec = pl.BlockSpec((tok, HEADS), lambda h: (0, 0))
    in_specs = [pl.BlockSpec(memory_space=pltpu.SMEM), q_spec]
    in_specs += [k_spec] * nblk + [v_spec] * nblk
    args = [valid, queries, *k_blocks, *v_blocks]
    if not first:
        in_specs += [stat_spec, stat_spec, q_spec]
        args += list(state)
    if last:
        out_specs = q_spec
        out_shape = jax.ShapeDtypeStruct(queries.shape, queries.dtype)
    else:
        out_specs = [stat_spec, stat_spec, q_spec]
        out_shape = [
            jax.ShapeDtypeStruct((tok, HEADS), jnp.float32),
            jax.ShapeDtypeStruct((tok, HEADS), jnp.float32),
            jax.ShapeDtypeStruct(queries.shape, jnp.float32),
        ]
    flops = 4 * HEADS * tok * tok * nblk * HEAD_DIM
    nbytes = 2 * queries.size * (2 if last else 1) + 4 * nblk * k_blocks[0].size
    nbytes += (0 if first else 4 * queries.size) + (0 if last else 4 * queries.size)
    return pl.pallas_call(
        functools.partial(step_kernel, tuple(kinds), first, last),
        grid=(KV_HEADS,),
        in_specs=in_specs,
        out_specs=out_specs,
        out_shape=out_shape,
        cost_estimate=pl.CostEstimate(
            flops=flops, transcendentals=HEADS * tok * tok * nblk, bytes_accessed=nbytes
        ),
    )(*args)


def shifted(x, axis, pairs):
    return lax.ppermute(x, axis, pairs)


def flags(*conds):
    return jnp.stack([c.astype(jnp.int32) for c in conds])


def body(queries, keys, values):
    axis = ("blk", "grp")
    n = lax.axis_size(axis)
    d = lax.axis_index(axis)
    odd = (d % 2) == 1
    own = (keys, values)
    ahead2 = [(i, i + 2) for i in range(n) if i + 2 < n]
    x1 = shifted(own, axis, ahead2)
    y1 = shifted(own, axis, [(i, i + 1) for i in range(0, n, 2)])
    x2 = shifted(x1, axis, ahead2)
    y2 = shifted(x1, axis, [(i, i ^ 1) for i in range(n)])
    y3 = shifted(x2, axis, [(i, i - 1) for i in range(1, n, 2)])

    first = [own, x1, y1]
    v1 = flags(d >= 0, d >= 2, odd)
    state = attend_step(
        (LOWER, WHOLE, WHOLE), True, False, v1, queries,
        [b[0] for b in first], [b[1] for b in first], None,
    )
    rest = [x2, y2, y3]
    v2 = flags(d >= 4, d >= jnp.where(odd, 3, 1), jnp.logical_not(odd) & (d >= 3))
    return attend_step(
        (UPPER, WHOLE, WHOLE), False, True, v2, queries,
        [b[0] for b in rest], [b[1] for b in rest], state,
    )


def solution(mesh):
    placed = (P(("blk", "grp"), None), P(("blk", "grp"), None), P(("blk", "grp"), None))
    return jax.shard_map(
        body, mesh=mesh, in_specs=placed, out_specs=P(("blk", "grp"), None), check_vma=False
    )
```

```python
import jax
import jax.numpy as jnp
from jax import lax
from jax.experimental import pallas as pl
from jax.experimental.pallas import tpu as pltpu
from jax.sharding import PartitionSpec as P

HEADS = 16
KV_HEADS = 8
HEAD_DIM = 128
WINDOW = 1024
NEG = -1e30


def from_behind(x, axis, by):
    peers = lax.axis_size(axis)
    pairs = [(i, i + by) for i in range(peers) if 0 <= i + by < peers]
    return lax.ppermute(x, axis, pairs)


def attend_kernel(valid_ref, q_ref, *refs):
    nblk = (len(refs) - 1) // 2
    k_refs, v_refs, o_ref = refs[:nblk], refs[nblk:2 * nblk], refs[-1]
    tok = q_ref.shape[0]
    row = lax.broadcasted_iota(jnp.int32, (tok, tok), 0)
    col = lax.broadcasted_iota(jnp.int32, (tok, tok), 1)
    group = HEADS // KV_HEADS
    for a in range(group):
        qa = q_ref[:, a * HEAD_DIM:(a + 1) * HEAD_DIM]
        scores = []
        for j in range(nblk):
            s = lax.dot_general(
                qa, k_refs[j][...], (((1,), (1,)), ((), ())),
                preferred_element_type=jnp.float32,
            ) * HEAD_DIM ** (-0.5)
            if j == 0:
                s = jnp.where((col > row) & (valid_ref[0] > 0), s, NEG)
            elif j == nblk - 1:
                s = jnp.where(col <= row, s, NEG)
            else:
                s = jnp.where(valid_ref[j] > 0, s, NEG)
            scores.append(s)
        largest = scores[0].max(axis=1, keepdims=True)
        for s in scores[1:]:
            largest = jnp.maximum(largest, s.max(axis=1, keepdims=True))
        expos = [jnp.exp(s - largest) for s in scores]
        total = expos[0].sum(axis=1, keepdims=True)
        for e in expos[1:]:
            total = total + e.sum(axis=1, keepdims=True)
        inv = 1.0 / total
        out = None
        for j in range(nblk):
            w = (expos[j] * inv).astype(jnp.bfloat16)
            part = jnp.dot(w, v_refs[j][...], preferred_element_type=jnp.float32)
            out = part if out is None else out + part
        o_ref[:, a * HEAD_DIM:(a + 1) * HEAD_DIM] = out.astype(o_ref.dtype)


def attend(valid, queries, k_blocks, v_blocks):
    tok = queries.shape[0]
    group = HEADS // KV_HEADS
    nblk = len(k_blocks)
    k_spec = pl.BlockSpec((tok, HEAD_DIM), lambda h: (0, h))
    v_spec = pl.BlockSpec((tok, HEAD_DIM), lambda h: (0, KV_HEADS + h))
    q_spec = pl.BlockSpec((tok, group * HEAD_DIM), lambda h: (0, h))
    flops = 4 * HEADS * tok * tok * nblk * HEAD_DIM
    nbytes = 2 * (2 * queries.size + nblk * k_blocks[0].size)
    return pl.pallas_call(
        attend_kernel,
        grid=(KV_HEADS,),
        in_specs=[pl.BlockSpec(memory_space=pltpu.SMEM), q_spec]
        + [k_spec] * nblk + [v_spec] * nblk,
        out_specs=q_spec,
        out_shape=jax.ShapeDtypeStruct(queries.shape, queries.dtype),
        cost_estimate=pl.CostEstimate(
            flops=flops, transcendentals=HEADS * tok * tok * nblk, bytes_accessed=nbytes
        ),
    )(valid, queries, *k_blocks, *v_blocks)


def attend_kv(valid, queries, kv_blocks):
    return attend(valid, queries, kv_blocks, kv_blocks)


def shifted(x, axis, pairs):
    return lax.ppermute(x, axis, pairs)


def body(queries, keys, values):
    axis = ("blk", "grp")
    n = lax.axis_size(axis)
    block_index = lax.axis_index(axis)
    own = jnp.concatenate([keys, values], axis=1)
    tok = own.shape[0]
    ahead2 = [(i, i + 2) for i in range(n) if i + 2 < n]
    pairs = [[i, i + 1] for i in range(0, lax.axis_size("grp"), 2)]

    def pair_gather(x):
        return lax.all_gather(x, "grp", axis_index_groups=pairs, axis=0, tiled=True)

    x1 = shifted(own, axis, ahead2)
    y1 = pair_gather(own)
    x2 = shifted(x1, axis, ahead2)
    y2 = pair_gather(x1)
    y3 = pair_gather(x2)
    odd = (block_index % 2) == 1
    b1 = jnp.where(odd, y1[:tok], y2[tok:])
    b3 = jnp.where(odd, y2[:tok], y3[tok:])
    back_blocks = WINDOW // queries.shape[0]
    nblk = back_blocks + 1
    valid = (block_index + jnp.arange(nblk, dtype=jnp.int32) >= back_blocks).astype(jnp.int32)
    return attend_kv(valid, queries, [x2, b3, x1, b1, own])


def solution(mesh):
    placed = (P(("blk", "grp"), None), P(("blk", "grp"), None), P(("blk", "grp"), None))
    return jax.shard_map(
        body, mesh=mesh, in_specs=placed, out_specs=P(("blk", "grp"), None), check_vma=False
    )
```

```python
import jax
import jax.numpy as jnp
from jax import lax
from jax.experimental import pallas as pl
from jax.experimental.pallas import tpu as pltpu
from jax.sharding import PartitionSpec as P

HEADS = 16
KV_HEADS = 8
HEAD_DIM = 128
WINDOW = 1024
NEG = -1e30


def from_behind(x, axis, by):
    peers = lax.axis_size(axis)
    pairs = [(i, i + by) for i in range(peers) if 0 <= i + by < peers]
    return lax.ppermute(x, axis, pairs)


def attend_kernel(valid_ref, q_ref, *refs):
    nblk = (len(refs) - 1) // 2
    k_refs, v_refs, o_ref = refs[:nblk], refs[nblk:2 * nblk], refs[-1]
    tok = q_ref.shape[0]
    row = lax.broadcasted_iota(jnp.int32, (tok, tok), 0)
    col = lax.broadcasted_iota(jnp.int32, (tok, tok), 1)
    group = HEADS // KV_HEADS
    for a in range(group):
        qa = q_ref[:, a * HEAD_DIM:(a + 1) * HEAD_DIM]
        scores = []
        for j in range(nblk):
            s = lax.dot_general(
                qa, k_refs[j][...], (((1,), (1,)), ((), ())),
                preferred_element_type=jnp.float32,
            ) * HEAD_DIM ** (-0.5)
            if j == 0:
                s = jnp.where((col > row) & (valid_ref[0] > 0), s, NEG)
            elif j == nblk - 1:
                s = jnp.where(col <= row, s, NEG)
            else:
                s = jnp.where(valid_ref[j] > 0, s, NEG)
            scores.append(s)
        largest = scores[0].max(axis=1, keepdims=True)
        for s in scores[1:]:
            largest = jnp.maximum(largest, s.max(axis=1, keepdims=True))
        expos = [jnp.exp(s - largest) for s in scores]
        total = expos[0].sum(axis=1, keepdims=True)
        for e in expos[1:]:
            total = total + e.sum(axis=1, keepdims=True)
        inv = 1.0 / total
        out = None
        for j in range(nblk):
            w = (expos[j] * inv).astype(jnp.bfloat16)
            part = jnp.dot(w, v_refs[j][...], preferred_element_type=jnp.float32)
            out = part if out is None else out + part
        o_ref[:, a * HEAD_DIM:(a + 1) * HEAD_DIM] = out.astype(o_ref.dtype)


def attend(valid, queries, k_blocks, v_blocks):
    tok = queries.shape[0]
    group = HEADS // KV_HEADS
    nblk = len(k_blocks)
    kv_spec = pl.BlockSpec((tok, HEAD_DIM), lambda h: (0, h))
    q_spec = pl.BlockSpec((tok, group * HEAD_DIM), lambda h: (0, h))
    flops = 4 * HEADS * tok * tok * nblk * HEAD_DIM
    nbytes = 2 * (2 * queries.size + 2 * nblk * k_blocks[0].size)
    return pl.pallas_call(
        attend_kernel,
        grid=(KV_HEADS,),
        in_specs=[pl.BlockSpec(memory_space=pltpu.SMEM), q_spec]
        + [kv_spec] * (2 * nblk),
        out_specs=q_spec,
        out_shape=jax.ShapeDtypeStruct(queries.shape, queries.dtype),
        cost_estimate=pl.CostEstimate(
            flops=flops, transcendentals=HEADS * tok * tok * nblk, bytes_accessed=nbytes
        ),
    )(valid, queries, *k_blocks, *v_blocks)


def shifted(x, axis, pairs):
    return lax.ppermute(x, axis, pairs)


def body(queries, keys, values):
    axis = ("blk", "grp")
    n = lax.axis_size(axis)
    block_index = lax.axis_index(axis)
    own = (keys, values)
    ahead2 = [(i, i + 2) for i in range(n) if i + 2 < n]
    x1 = shifted(own, axis, ahead2)
    y1 = shifted(own, axis, [(i, i + 1) for i in range(0, n, 2)])
    x2 = shifted(x1, axis, ahead2)
    x1_fenced = tuple(lax.optimization_barrier((a, b))[0] for a, b in zip(x1, y1))
    y2 = shifted(x1_fenced, axis, [(i, i ^ 1) for i in range(n)])
    y3 = shifted(x2, axis, [(i, i - 1) for i in range(1, n, 2)])
    odd = (block_index % 2) == 1
    b1 = [jnp.where(odd, a, b) for a, b in zip(y1, y2)]
    b3 = [jnp.where(odd, a, b) for a, b in zip(y2, y3)]
    back_blocks = WINDOW // queries.shape[0]
    nblk = back_blocks + 1
    valid = (block_index + jnp.arange(nblk, dtype=jnp.int32) >= back_blocks).astype(jnp.int32)
    k_blocks = [x2[0], b3[0], x1[0], b1[0], keys]
    v_blocks = [x2[1], b3[1], x1[1], b1[1], values]
    return attend(valid, queries, k_blocks, v_blocks)


def solution(mesh):
    placed = (P(("blk", "grp"), None), P(("blk", "grp"), None), P(("blk", "grp"), None))
    return jax.shard_map(
        body, mesh=mesh, in_specs=placed, out_specs=P(("blk", "grp"), None), check_vma=False
    )
```

```python
import jax
import jax.numpy as jnp
from jax import lax
from jax.experimental import pallas as pl
from jax.experimental.pallas import tpu as pltpu
from jax.sharding import PartitionSpec as P

HEADS = 16
KV_HEADS = 8
HEAD_DIM = 128
WINDOW = 1024
NEG = -1e30


def from_behind(x, axis, by):
    peers = lax.axis_size(axis)
    pairs = [(i, i + by) for i in range(peers) if 0 <= i + by < peers]
    return lax.ppermute(x, axis, pairs)


def attend_kernel(valid_ref, q_ref, *refs):
    nblk = (len(refs) - 1) // 2
    k_refs, v_refs, o_ref = refs[:nblk], refs[nblk:2 * nblk], refs[-1]
    tok = q_ref.shape[0]
    row = lax.broadcasted_iota(jnp.int32, (tok, tok), 0)
    col = lax.broadcasted_iota(jnp.int32, (tok, tok), 1)
    group = HEADS // KV_HEADS
    for a in range(group):
        qa = q_ref[:, a * HEAD_DIM:(a + 1) * HEAD_DIM]
        scores = []
        for j in range(nblk):
            s = lax.dot_general(
                qa, k_refs[j][...], (((1,), (1,)), ((), ())),
                preferred_element_type=jnp.float32,
            ) * HEAD_DIM ** (-0.5)
            if j == 0:
                s = jnp.where((col > row) & (valid_ref[0] > 0), s, NEG)
            elif j == nblk - 1:
                s = jnp.where(col <= row, s, NEG)
            else:
                s = jnp.where(valid_ref[j] > 0, s, NEG)
            scores.append(s)
        largest = scores[0].max(axis=1, keepdims=True)
        for s in scores[1:]:
            largest = jnp.maximum(largest, s.max(axis=1, keepdims=True))
        expos = [jnp.exp(s - largest) for s in scores]
        total = expos[0].sum(axis=1, keepdims=True)
        for e in expos[1:]:
            total = total + e.sum(axis=1, keepdims=True)
        inv = 1.0 / total
        out = None
        for j in range(nblk):
            w = (expos[j] * inv).astype(jnp.bfloat16)
            part = jnp.dot(w, v_refs[j][...], preferred_element_type=jnp.float32)
            out = part if out is None else out + part
        o_ref[:, a * HEAD_DIM:(a + 1) * HEAD_DIM] = out.astype(o_ref.dtype)


def attend(valid, queries, k_blocks, v_blocks):
    tok = queries.shape[0]
    group = HEADS // KV_HEADS
    nblk = len(k_blocks)
    kv_spec = pl.BlockSpec((tok, HEAD_DIM), lambda h: (0, h))
    q_spec = pl.BlockSpec((tok, group * HEAD_DIM), lambda h: (0, h))
    flops = 4 * HEADS * tok * tok * nblk * HEAD_DIM
    nbytes = 2 * (2 * queries.size + 2 * nblk * k_blocks[0].size)
    return pl.pallas_call(
        attend_kernel,
        grid=(KV_HEADS,),
        in_specs=[pl.BlockSpec(memory_space=pltpu.SMEM), q_spec]
        + [kv_spec] * (2 * nblk),
        out_specs=q_spec,
        out_shape=jax.ShapeDtypeStruct(queries.shape, queries.dtype),
        cost_estimate=pl.CostEstimate(
            flops=flops, transcendentals=HEADS * tok * tok * nblk, bytes_accessed=nbytes
        ),
    )(valid, queries, *k_blocks, *v_blocks)


def shifted(x, axis, pairs):
    return lax.ppermute(x, axis, pairs)


def body(queries, keys, values):
    axis = ("blk", "grp")
    n = lax.axis_size(axis)
    block_index = lax.axis_index(axis)
    own = (keys, values)
    plane = 2 * lax.axis_size("grp")

    def crossing(t):
        return t % plane < 2

    ahead2 = [(i, i + 2) for i in range(n) if i + 2 < n]
    x1 = shifted(own, axis, ahead2)
    y1 = shifted(own, axis, [(i, i + 1) for i in range(0, n, 2)])
    far = shifted(own, axis, [(i, i + 4) for i in range(n) if i + 4 < n and crossing(i + 4)])
    x2 = shifted(x1, axis, [(i, i + 2) for i in range(n) if i + 2 < n and not crossing(i + 2)])
    first_two = (block_index % plane) < 2
    b4 = [jnp.where(first_two, a, b) for a, b in zip(far, x2)]
    y2 = shifted(x1, axis, [(i, i ^ 1) for i in range(n)])
    y3 = shifted(b4, axis, [(i, i - 1) for i in range(1, n, 2)])
    odd = (block_index % 2) == 1
    b1 = [jnp.where(odd, a, b) for a, b in zip(y1, y2)]
    b3 = [jnp.where(odd, a, b) for a, b in zip(y2, y3)]
    back_blocks = WINDOW // queries.shape[0]
    nblk = back_blocks + 1
    valid = (block_index + jnp.arange(nblk, dtype=jnp.int32) >= back_blocks).astype(jnp.int32)
    k_blocks = [b4[0], b3[0], x1[0], b1[0], keys]
    v_blocks = [b4[1], b3[1], x1[1], b1[1], values]
    return attend(valid, queries, k_blocks, v_blocks)


def solution(mesh):
    placed = (P(("blk", "grp"), None), P(("blk", "grp"), None), P(("blk", "grp"), None))
    return jax.shard_map(
        body, mesh=mesh, in_specs=placed, out_specs=P(("blk", "grp"), None), check_vma=False
    )
```

```python
import functools

import jax
import jax.numpy as jnp
from jax import lax
from jax.experimental import pallas as pl
from jax.experimental.pallas import tpu as pltpu
from jax.sharding import PartitionSpec as P

HEADS = 16
KV_HEADS = 8
HEAD_DIM = 128
WINDOW = 1024
NEG = -1e30


def from_behind(x, axis, by):
    peers = lax.axis_size(axis)
    pairs = [(i, i + by) for i in range(peers) if 0 <= i + by < peers]
    return lax.ppermute(x, axis, pairs)


def attend_kernel(slots, valid_ref, q_ref, *refs):
    nref = (len(refs) - 1) // 2
    k_refs, v_refs, o_ref = refs[:nref], refs[nref:2 * nref], refs[-1]
    nblk = len(slots)
    odd = valid_ref[nblk] > 0

    def load(which, slot):
        if isinstance(slot, tuple):
            return jnp.where(odd, which[slot[0]][...], which[slot[1]][...])
        return which[slot][...]

    tok = q_ref.shape[0]
    row = lax.broadcasted_iota(jnp.int32, (tok, tok), 0)
    col = lax.broadcasted_iota(jnp.int32, (tok, tok), 1)
    group = HEADS // KV_HEADS
    keys = [load(k_refs, s) for s in slots]
    vals = [load(v_refs, s) for s in slots]
    for a in range(group):
        qa = q_ref[:, a * HEAD_DIM:(a + 1) * HEAD_DIM]
        scores = []
        for j in range(nblk):
            s = lax.dot_general(
                qa, keys[j], (((1,), (1,)), ((), ())),
                preferred_element_type=jnp.float32,
            ) * HEAD_DIM ** (-0.5)
            if j == 0:
                s = jnp.where((col > row) & (valid_ref[0] > 0), s, NEG)
            elif j == nblk - 1:
                s = jnp.where(col <= row, s, NEG)
            else:
                s = jnp.where(valid_ref[j] > 0, s, NEG)
            scores.append(s)
        largest = scores[0].max(axis=1, keepdims=True)
        for s in scores[1:]:
            largest = jnp.maximum(largest, s.max(axis=1, keepdims=True))
        expos = [jnp.exp(s - largest) for s in scores]
        total = expos[0].sum(axis=1, keepdims=True)
        for e in expos[1:]:
            total = total + e.sum(axis=1, keepdims=True)
        inv = 1.0 / total
        out = None
        for j in range(nblk):
            w = (expos[j] * inv).astype(jnp.bfloat16)
            part = jnp.dot(w, vals[j], preferred_element_type=jnp.float32)
            out = part if out is None else out + part
        o_ref[:, a * HEAD_DIM:(a + 1) * HEAD_DIM] = out.astype(o_ref.dtype)


def attend(slots, valid, queries, k_arrays, v_arrays):
    tok = queries.shape[0]
    group = HEADS // KV_HEADS
    nblk = len(slots)
    nref = len(k_arrays)
    kv_spec = pl.BlockSpec((tok, HEAD_DIM), lambda h: (0, h))
    q_spec = pl.BlockSpec((tok, group * HEAD_DIM), lambda h: (0, h))
    flops = 4 * HEADS * tok * tok * nblk * HEAD_DIM
    nbytes = 2 * (2 * queries.size + 2 * nref * k_arrays[0].size)
    return pl.pallas_call(
        functools.partial(attend_kernel, tuple(slots)),
        grid=(KV_HEADS,),
        in_specs=[pl.BlockSpec(memory_space=pltpu.SMEM), q_spec]
        + [kv_spec] * (2 * nref),
        out_specs=q_spec,
        out_shape=jax.ShapeDtypeStruct(queries.shape, queries.dtype),
        cost_estimate=pl.CostEstimate(
            flops=flops, transcendentals=HEADS * tok * tok * nblk, bytes_accessed=nbytes
        ),
    )(valid, queries, *k_arrays, *v_arrays)


def shifted(x, axis, pairs):
    return lax.ppermute(x, axis, pairs)


def body(queries, keys, values):
    axis = ("blk", "grp")
    n = lax.axis_size(axis)
    block_index = lax.axis_index(axis)
    own = (keys, values)
    plane = 2 * lax.axis_size("grp")

    def crossing(t):
        return t % plane < 2

    ahead2 = [(i, i + 2) for i in range(n) if i + 2 < n]
    x1 = shifted(own, axis, ahead2)
    y1 = shifted(own, axis, [(i, i + 1) for i in range(0, n, 2)])
    far = shifted(own, axis, [(i, i + 4) for i in range(n) if i + 4 < n and crossing(i + 4)])
    x2 = shifted(x1, axis, [(i, i + 2) for i in range(n) if i + 2 < n and not crossing(i + 2)])
    first_two = (block_index % plane) < 2
    b4 = [jnp.where(first_two, a, b) for a, b in zip(far, x2)]
    y2 = shifted(x1, axis, [(i, i ^ 1) for i in range(n)])
    y3 = shifted(b4, axis, [(i, i - 1) for i in range(1, n, 2)])
    odd = (block_index % 2) == 1
    back_blocks = WINDOW // queries.shape[0]
    nblk = back_blocks + 1
    valid = (block_index + jnp.arange(nblk, dtype=jnp.int32) >= back_blocks).astype(jnp.int32)
    valid = jnp.concatenate([valid, odd.astype(jnp.int32).reshape(1)])
    slots = (0, (2, 3), 4, (1, 2), 5)
    k_arrays = [b4[0], y1[0], y2[0], y3[0], x1[0], keys]
    v_arrays = [b4[1], y1[1], y2[1], y3[1], x1[1], values]
    return attend(slots, valid, queries, k_arrays, v_arrays)


def solution(mesh):
    placed = (P(("blk", "grp"), None), P(("blk", "grp"), None), P(("blk", "grp"), None))
    return jax.shard_map(
        body, mesh=mesh, in_specs=placed, out_specs=P(("blk", "grp"), None), check_vma=False
    )
```

```python
import jax
import jax.numpy as jnp
from jax import lax
from jax.experimental import pallas as pl
from jax.experimental.pallas import tpu as pltpu
from jax.sharding import PartitionSpec as P

HEADS = 16
KV_HEADS = 8
HEAD_DIM = 128
WINDOW = 1024
NEG = -1e30


def from_behind(x, axis, by):
    peers = lax.axis_size(axis)
    pairs = [(i, i + by) for i in range(peers) if 0 <= i + by < peers]
    return lax.ppermute(x, axis, pairs)


def attend_kernel(valid_ref, q_ref, *refs):
    nblk = (len(refs) - 1) // 2
    k_refs, v_refs, o_ref = refs[:nblk], refs[nblk:2 * nblk], refs[-1]
    tok = q_ref.shape[0]
    row = lax.broadcasted_iota(jnp.int32, (tok, tok), 0)
    col = lax.broadcasted_iota(jnp.int32, (tok, tok), 1)
    group = HEADS // KV_HEADS
    for a in range(group):
        qa = q_ref[:, a * HEAD_DIM:(a + 1) * HEAD_DIM]
        scores = []
        for j in range(nblk):
            s = lax.dot_general(
                qa, k_refs[j][...], (((1,), (1,)), ((), ())),
                preferred_element_type=jnp.float32,
            ) * HEAD_DIM ** (-0.5)
            if j == 0:
                s = jnp.where((col > row) & (valid_ref[0] > 0), s, NEG)
            elif j == nblk - 1:
                s = jnp.where(col <= row, s, NEG)
            else:
                s = jnp.where(valid_ref[j] > 0, s, NEG)
            scores.append(s)
        largest = scores[0].max(axis=1, keepdims=True)
        for s in scores[1:]:
            largest = jnp.maximum(largest, s.max(axis=1, keepdims=True))
        expos = [jnp.exp(s - largest) for s in scores]
        total = expos[0].sum(axis=1, keepdims=True)
        for e in expos[1:]:
            total = total + e.sum(axis=1, keepdims=True)
        inv = 1.0 / total
        out = None
        for j in range(nblk):
            w = (expos[j] * inv).astype(jnp.bfloat16)
            part = jnp.dot(w, v_refs[j][...], preferred_element_type=jnp.float32)
            out = part if out is None else out + part
        o_ref[:, a * HEAD_DIM:(a + 1) * HEAD_DIM] = out.astype(o_ref.dtype)


def attend(valid, queries, k_blocks, v_blocks):
    tok = queries.shape[0]
    group = HEADS // KV_HEADS
    nblk = len(k_blocks)
    kv_spec = pl.BlockSpec((tok, HEAD_DIM), lambda h: (0, h))
    q_spec = pl.BlockSpec((tok, group * HEAD_DIM), lambda h: (0, h))
    flops = 4 * HEADS * tok * tok * nblk * HEAD_DIM
    nbytes = 2 * (2 * queries.size + 2 * nblk * k_blocks[0].size)
    return pl.pallas_call(
        attend_kernel,
        grid=(KV_HEADS,),
        in_specs=[pl.BlockSpec(memory_space=pltpu.SMEM), q_spec]
        + [kv_spec] * (2 * nblk),
        out_specs=q_spec,
        out_shape=jax.ShapeDtypeStruct(queries.shape, queries.dtype),
        cost_estimate=pl.CostEstimate(
            flops=flops, transcendentals=HEADS * tok * tok * nblk, bytes_accessed=nbytes
        ),
    )(valid, queries, *k_blocks, *v_blocks)


def shifted(x, axis, pairs):
    return lax.ppermute(x, axis, pairs)


def body(queries, keys, values):
    axis = ("blk", "grp")
    n = lax.axis_size(axis)
    block_index = lax.axis_index(axis)
    own = (keys, values)
    plane = 2 * lax.axis_size("grp")

    def crossing(t):
        return t % plane < 2

    ahead2 = [(i, i + 2) for i in range(n) if i + 2 < n]
    x1_near = shifted(own, axis, [(i, i + 2) for i in range(n) if i + 2 < n and not crossing(i + 2)])
    x1_far = shifted(own, axis, [(i, i + 2) for i in range(n) if i + 2 < n and crossing(i + 2)])
    y1 = shifted(own, axis, [(i, i + 1) for i in range(0, n, 2)])
    first_two = (block_index % plane) < 2
    x1 = [jnp.where(first_two, a, b) for a, b in zip(x1_far, x1_near)]
    far = shifted(own, axis, [(i, i + 4) for i in range(n) if i + 4 < n and crossing(i + 4)])
    x2 = shifted(x1, axis, [(i, i + 2) for i in range(n) if i + 2 < n and not crossing(i + 2)])
    b4 = [jnp.where(first_two, a, b) for a, b in zip(far, x2)]
    y2 = shifted(x1, axis, [(i, i ^ 1) for i in range(n)])
    y3 = shifted(b4, axis, [(i, i - 1) for i in range(1, n, 2)])
    odd = (block_index % 2) == 1
    b1 = [jnp.where(odd, a, b) for a, b in zip(y1, y2)]
    b3 = [jnp.where(odd, a, b) for a, b in zip(y2, y3)]
    back_blocks = WINDOW // queries.shape[0]
    nblk = back_blocks + 1
    valid = (block_index + jnp.arange(nblk, dtype=jnp.int32) >= back_blocks).astype(jnp.int32)
    k_blocks = [b4[0], b3[0], x1[0], b1[0], keys]
    v_blocks = [b4[1], b3[1], x1[1], b1[1], values]
    return attend(valid, queries, k_blocks, v_blocks)


def solution(mesh):
    placed = (P(("blk", "grp"), None), P(("blk", "grp"), None), P(("blk", "grp"), None))
    return jax.shard_map(
        body, mesh=mesh, in_specs=placed, out_specs=P(("blk", "grp"), None), check_vma=False
    )
```

```python
import jax
import jax.numpy as jnp
from jax import lax
from jax.experimental import pallas as pl
from jax.experimental.pallas import tpu as pltpu
from jax.sharding import PartitionSpec as P

HEADS = 16
KV_HEADS = 8
HEAD_DIM = 128
WINDOW = 1024
NEG = -1e30


def from_behind(x, axis, by):
    peers = lax.axis_size(axis)
    pairs = [(i, i + by) for i in range(peers) if 0 <= i + by < peers]
    return lax.ppermute(x, axis, pairs)


def attend_kernel(valid_ref, q_ref, *refs):
    nblk = (len(refs) - 1) // 2
    k_refs, v_refs, o_ref = refs[:nblk], refs[nblk:2 * nblk], refs[-1]
    tok = q_ref.shape[0]
    row = lax.broadcasted_iota(jnp.int32, (tok, tok), 0)
    col = lax.broadcasted_iota(jnp.int32, (tok, tok), 1)
    group = HEADS // KV_HEADS
    for a in range(group):
        qa = q_ref[:, a * HEAD_DIM:(a + 1) * HEAD_DIM]
        scores = []
        for j in range(nblk):
            s = lax.dot_general(
                qa, k_refs[j][...], (((1,), (1,)), ((), ())),
                preferred_element_type=jnp.float32,
            ) * HEAD_DIM ** (-0.5)
            if j == 0:
                s = jnp.where((col > row) & (valid_ref[0] > 0), s, NEG)
            elif j == nblk - 1:
                s = jnp.where(col <= row, s, NEG)
            else:
                s = jnp.where(valid_ref[j] > 0, s, NEG)
            scores.append(s)
        largest = scores[0].max(axis=1, keepdims=True)
        for s in scores[1:]:
            largest = jnp.maximum(largest, s.max(axis=1, keepdims=True))
        expos = [jnp.exp(s - largest) for s in scores]
        total = expos[0].sum(axis=1, keepdims=True)
        for e in expos[1:]:
            total = total + e.sum(axis=1, keepdims=True)
        inv = 1.0 / total
        out = None
        for j in range(nblk):
            w = (expos[j] * inv).astype(jnp.bfloat16)
            part = jnp.dot(w, v_refs[j][...], preferred_element_type=jnp.float32)
            out = part if out is None else out + part
        o_ref[:, a * HEAD_DIM:(a + 1) * HEAD_DIM] = out.astype(o_ref.dtype)


def attend(valid, queries, k_blocks, v_blocks):
    tok = queries.shape[0]
    group = HEADS // KV_HEADS
    nblk = len(k_blocks)
    kv_spec = pl.BlockSpec((tok, HEAD_DIM), lambda h: (0, h))
    q_spec = pl.BlockSpec((tok, group * HEAD_DIM), lambda h: (0, h))
    flops = 4 * HEADS * tok * tok * nblk * HEAD_DIM
    nbytes = 2 * (2 * queries.size + 2 * nblk * k_blocks[0].size)
    return pl.pallas_call(
        attend_kernel,
        grid=(KV_HEADS,),
        in_specs=[pl.BlockSpec(memory_space=pltpu.SMEM), q_spec]
        + [kv_spec] * (2 * nblk),
        out_specs=q_spec,
        out_shape=jax.ShapeDtypeStruct(queries.shape, queries.dtype),
        cost_estimate=pl.CostEstimate(
            flops=flops, transcendentals=HEADS * tok * tok * nblk, bytes_accessed=nbytes
        ),
    )(valid, queries, *k_blocks, *v_blocks)


def shifted(x, axis, pairs):
    return lax.ppermute(x, axis, pairs)


def body(queries, keys, values):
    axis = ("blk", "grp")
    n = lax.axis_size(axis)
    block_index = lax.axis_index(axis)
    own = (keys, values)
    plane = 2 * lax.axis_size("grp")
    back = WINDOW // queries.shape[0]

    def crossing(t):
        return t % plane < back

    ahead2 = [(i, i + 2) for i in range(n) if i + 2 < n]
    x1 = shifted(own, axis, ahead2)
    y1 = shifted(own, axis, [(i, i + 1) for i in range(0, n, 2)])
    far = shifted(own, axis, [(i, i + 4) for i in range(n) if i + 4 < n and crossing(i + 4)])
    x2 = shifted(x1, axis, [(i, i + 2) for i in range(n) if i + 2 < n and not crossing(i + 2)])
    first_few = (block_index % plane) < back
    b4 = [jnp.where(first_few, a, b) for a, b in zip(far, x2)]
    y2 = shifted(x1, axis, [(i, i ^ 1) for i in range(n)])
    y3 = shifted(b4, axis, [(i, i - 1) for i in range(1, n, 2)])
    odd = (block_index % 2) == 1
    b1 = [jnp.where(odd, a, b) for a, b in zip(y1, y2)]
    b3 = [jnp.where(odd, a, b) for a, b in zip(y2, y3)]
    back_blocks = WINDOW // queries.shape[0]
    nblk = back_blocks + 1
    valid = (block_index + jnp.arange(nblk, dtype=jnp.int32) >= back_blocks).astype(jnp.int32)
    k_blocks = [b4[0], b3[0], x1[0], b1[0], keys]
    v_blocks = [b4[1], b3[1], x1[1], b1[1], values]
    return attend(valid, queries, k_blocks, v_blocks)


def solution(mesh):
    placed = (P(("blk", "grp"), None), P(("blk", "grp"), None), P(("blk", "grp"), None))
    return jax.shard_map(
        body, mesh=mesh, in_specs=placed, out_specs=P(("blk", "grp"), None), check_vma=False
    )
```

```python
import jax
import jax.numpy as jnp
from jax import lax
from jax.experimental import pallas as pl
from jax.experimental.pallas import tpu as pltpu
from jax.sharding import PartitionSpec as P

HEADS = 16
KV_HEADS = 8
HEAD_DIM = 128
WINDOW = 1024
NEG = -1e30


def from_behind(x, axis, by):
    peers = lax.axis_size(axis)
    pairs = [(i, i + by) for i in range(peers) if 0 <= i + by < peers]
    return lax.ppermute(x, axis, pairs)


def attend_kernel(valid_ref, q_ref, *refs):
    nblk = (len(refs) - 1) // 2
    k_refs, v_refs, o_ref = refs[:nblk], refs[nblk:2 * nblk], refs[-1]
    tok = q_ref.shape[0]
    half = tok // 2
    group = HEADS // KV_HEADS
    for r in range(2):
        rows = slice(r * half, (r + 1) * half)
        spans = []
        for j in range(nblk):
            if j == 0 and r == 1:
                spans.append(slice(half, tok))
            elif j == nblk - 1 and r == 0:
                spans.append(slice(0, half))
            else:
                spans.append(slice(0, tok))
        for a in range(group):
            qa = q_ref[rows, a * HEAD_DIM:(a + 1) * HEAD_DIM]
            scores = []
            for j in range(nblk):
                cs = spans[j]
                width = cs.stop - cs.start
                s = lax.dot_general(
                    qa, k_refs[j][cs, :], (((1,), (1,)), ((), ())),
                    preferred_element_type=jnp.float32,
                ) * HEAD_DIM ** (-0.5)
                row = lax.broadcasted_iota(jnp.int32, (half, width), 0) + r * half
                col = lax.broadcasted_iota(jnp.int32, (half, width), 1) + cs.start
                if j == 0:
                    s = jnp.where((col > row) & (valid_ref[0] > 0), s, NEG)
                elif j == nblk - 1:
                    s = jnp.where(col <= row, s, NEG)
                else:
                    s = jnp.where(valid_ref[j] > 0, s, NEG)
                scores.append(s)
            largest = scores[0].max(axis=1, keepdims=True)
            for s in scores[1:]:
                largest = jnp.maximum(largest, s.max(axis=1, keepdims=True))
            expos = [jnp.exp(s - largest) for s in scores]
            total = expos[0].sum(axis=1, keepdims=True)
            for e in expos[1:]:
                total = total + e.sum(axis=1, keepdims=True)
            inv = 1.0 / total
            out = None
            for j in range(nblk):
                w = (expos[j] * inv).astype(jnp.bfloat16)
                part = jnp.dot(w, v_refs[j][spans[j], :], preferred_element_type=jnp.float32)
                out = part if out is None else out + part
            o_ref[rows, a * HEAD_DIM:(a + 1) * HEAD_DIM] = out.astype(o_ref.dtype)


def attend(valid, queries, k_blocks, v_blocks):
    tok = queries.shape[0]
    group = HEADS // KV_HEADS
    nblk = len(k_blocks)
    kv_spec = pl.BlockSpec((tok, HEAD_DIM), lambda h: (0, h))
    q_spec = pl.BlockSpec((tok, group * HEAD_DIM), lambda h: (0, h))
    flops = 4 * HEADS * tok * tok * nblk * HEAD_DIM
    nbytes = 2 * (2 * queries.size + 2 * nblk * k_blocks[0].size)
    return pl.pallas_call(
        attend_kernel,
        grid=(KV_HEADS,),
        in_specs=[pl.BlockSpec(memory_space=pltpu.SMEM), q_spec]
        + [kv_spec] * (2 * nblk),
        out_specs=q_spec,
        out_shape=jax.ShapeDtypeStruct(queries.shape, queries.dtype),
        cost_estimate=pl.CostEstimate(
            flops=flops, transcendentals=HEADS * tok * tok * nblk, bytes_accessed=nbytes
        ),
    )(valid, queries, *k_blocks, *v_blocks)


def shifted(x, axis, pairs):
    return lax.ppermute(x, axis, pairs)


def body(queries, keys, values):
    axis = ("blk", "grp")
    n = lax.axis_size(axis)
    block_index = lax.axis_index(axis)
    own = (keys, values)
    plane = 2 * lax.axis_size("grp")

    def crossing(t):
        return t % plane < 2

    ahead2 = [(i, i + 2) for i in range(n) if i + 2 < n]
    x1 = shifted(own, axis, ahead2)
    y1 = shifted(own, axis, [(i, i + 1) for i in range(0, n, 2)])
    far = shifted(own, axis, [(i, i + 4) for i in range(n) if i + 4 < n and crossing(i + 4)])
    x2 = shifted(x1, axis, [(i, i + 2) for i in range(n) if i + 2 < n and not crossing(i + 2)])
    first_two = (block_index % plane) < 2
    b4 = [jnp.where(first_two, a, b) for a, b in zip(far, x2)]
    y2 = shifted(x1, axis, [(i, i ^ 1) for i in range(n)])
    y3 = shifted(b4, axis, [(i, i - 1) for i in range(1, n, 2)])
    odd = (block_index % 2) == 1
    b1 = [jnp.where(odd, a, b) for a, b in zip(y1, y2)]
    b3 = [jnp.where(odd, a, b) for a, b in zip(y2, y3)]
    back_blocks = WINDOW // queries.shape[0]
    nblk = back_blocks + 1
    valid = (block_index + jnp.arange(nblk, dtype=jnp.int32) >= back_blocks).astype(jnp.int32)
    k_blocks = [b4[0], b3[0], x1[0], b1[0], keys]
    v_blocks = [b4[1], b3[1], x1[1], b1[1], values]
    return attend(valid, queries, k_blocks, v_blocks)


def solution(mesh):
    placed = (P(("blk", "grp"), None), P(("blk", "grp"), None), P(("blk", "grp"), None))
    return jax.shard_map(
        body, mesh=mesh, in_specs=placed, out_specs=P(("blk", "grp"), None), check_vma=False
    )
```

```python
import jax
import jax.numpy as jnp
from jax import lax
from jax.experimental import pallas as pl
from jax.experimental.pallas import tpu as pltpu
from jax.sharding import PartitionSpec as P

HEADS = 16
KV_HEADS = 8
HEAD_DIM = 128
WINDOW = 1024
NEG = -1e30


def from_behind(x, axis, by):
    peers = lax.axis_size(axis)
    pairs = [(i, i + by) for i in range(peers) if 0 <= i + by < peers]
    return lax.ppermute(x, axis, pairs)


def attend_kernel(valid_ref, q_ref, *refs):
    nblk = (len(refs) - 1) // 2
    k_refs, v_refs, o_ref = refs[:nblk], refs[nblk:2 * nblk], refs[-1]
    tok = q_ref.shape[0]
    group = HEADS // KV_HEADS
    q = jnp.concatenate(
        [q_ref[:, a * HEAD_DIM:(a + 1) * HEAD_DIM] for a in range(group)], axis=0
    )
    row = lax.broadcasted_iota(jnp.int32, (group * tok, tok), 0) % tok
    col = lax.broadcasted_iota(jnp.int32, (group * tok, tok), 1)
    scores = []
    for j in range(nblk):
        s = lax.dot_general(
            q, k_refs[j][...], (((1,), (1,)), ((), ())),
            preferred_element_type=jnp.float32,
        ) * HEAD_DIM ** (-0.5)
        if j == 0:
            s = jnp.where((col > row) & (valid_ref[0] > 0), s, NEG)
        elif j == nblk - 1:
            s = jnp.where(col <= row, s, NEG)
        else:
            s = jnp.where(valid_ref[j] > 0, s, NEG)
        scores.append(s)
    largest = scores[0].max(axis=1, keepdims=True)
    for s in scores[1:]:
        largest = jnp.maximum(largest, s.max(axis=1, keepdims=True))
    expos = [jnp.exp(s - largest) for s in scores]
    total = expos[0].sum(axis=1, keepdims=True)
    for e in expos[1:]:
        total = total + e.sum(axis=1, keepdims=True)
    inv = 1.0 / total
    out = None
    for j in range(nblk):
        w = (expos[j] * inv).astype(jnp.bfloat16)
        part = jnp.dot(w, v_refs[j][...], preferred_element_type=jnp.float32)
        out = part if out is None else out + part
    for a in range(group):
        o_ref[:, a * HEAD_DIM:(a + 1) * HEAD_DIM] = out[a * tok:(a + 1) * tok].astype(o_ref.dtype)


def attend(valid, queries, k_blocks, v_blocks):
    tok = queries.shape[0]
    group = HEADS // KV_HEADS
    nblk = len(k_blocks)
    kv_spec = pl.BlockSpec((tok, HEAD_DIM), lambda h: (0, h))
    q_spec = pl.BlockSpec((tok, group * HEAD_DIM), lambda h: (0, h))
    flops = 4 * HEADS * tok * tok * nblk * HEAD_DIM
    nbytes = 2 * (2 * queries.size + 2 * nblk * k_blocks[0].size)
    return pl.pallas_call(
        attend_kernel,
        grid=(KV_HEADS,),
        in_specs=[pl.BlockSpec(memory_space=pltpu.SMEM), q_spec]
        + [kv_spec] * (2 * nblk),
        out_specs=q_spec,
        out_shape=jax.ShapeDtypeStruct(queries.shape, queries.dtype),
        cost_estimate=pl.CostEstimate(
            flops=flops, transcendentals=HEADS * tok * tok * nblk, bytes_accessed=nbytes
        ),
    )(valid, queries, *k_blocks, *v_blocks)


def shifted(x, axis, pairs):
    return lax.ppermute(x, axis, pairs)


def body(queries, keys, values):
    axis = ("blk", "grp")
    n = lax.axis_size(axis)
    block_index = lax.axis_index(axis)
    own = (keys, values)
    plane = 2 * lax.axis_size("grp")

    def crossing(t):
        return t % plane < 2

    ahead2 = [(i, i + 2) for i in range(n) if i + 2 < n]
    x1 = shifted(own, axis, ahead2)
    y1 = shifted(own, axis, [(i, i + 1) for i in range(0, n, 2)])
    far = shifted(own, axis, [(i, i + 4) for i in range(n) if i + 4 < n and crossing(i + 4)])
    x2 = shifted(x1, axis, [(i, i + 2) for i in range(n) if i + 2 < n and not crossing(i + 2)])
    first_two = (block_index % plane) < 2
    b4 = [jnp.where(first_two, a, b) for a, b in zip(far, x2)]
    y2 = shifted(x1, axis, [(i, i ^ 1) for i in range(n)])
    y3 = shifted(b4, axis, [(i, i - 1) for i in range(1, n, 2)])
    odd = (block_index % 2) == 1
    b1 = [jnp.where(odd, a, b) for a, b in zip(y1, y2)]
    b3 = [jnp.where(odd, a, b) for a, b in zip(y2, y3)]
    back_blocks = WINDOW // queries.shape[0]
    nblk = back_blocks + 1
    valid = (block_index + jnp.arange(nblk, dtype=jnp.int32) >= back_blocks).astype(jnp.int32)
    k_blocks = [b4[0], b3[0], x1[0], b1[0], keys]
    v_blocks = [b4[1], b3[1], x1[1], b1[1], values]
    return attend(valid, queries, k_blocks, v_blocks)


def solution(mesh):
    placed = (P(("blk", "grp"), None), P(("blk", "grp"), None), P(("blk", "grp"), None))
    return jax.shard_map(
        body, mesh=mesh, in_specs=placed, out_specs=P(("blk", "grp"), None), check_vma=False
    )
```

```python
import jax
import jax.numpy as jnp
from jax import lax
from jax.experimental import pallas as pl
from jax.experimental.pallas import tpu as pltpu
from jax.sharding import PartitionSpec as P

HEADS = 16
KV_HEADS = 8
HEAD_DIM = 128
WINDOW = 1024
NEG = -1e30


def from_behind(x, axis, by):
    peers = lax.axis_size(axis)
    pairs = [(i, i + by) for i in range(peers) if 0 <= i + by < peers]
    return lax.ppermute(x, axis, pairs)


def attend_kernel(valid_ref, q_ref, *refs):
    nblk = (len(refs) - 1) // 2
    k_refs, v_refs, o_ref = refs[:nblk], refs[nblk:2 * nblk], refs[-1]
    tok = q_ref.shape[0]
    row = lax.broadcasted_iota(jnp.int32, (tok, tok), 0)
    col = lax.broadcasted_iota(jnp.int32, (tok, tok), 1)
    group = HEADS // KV_HEADS
    for a in range(group):
        qa = q_ref[:, a * HEAD_DIM:(a + 1) * HEAD_DIM]
        scores = []
        for j in range(nblk):
            s = lax.dot_general(
                qa, k_refs[j][...], (((1,), (1,)), ((), ())),
                preferred_element_type=jnp.float32,
            ) * HEAD_DIM ** (-0.5)
            if j == 0:
                s = jnp.where((col > row) & (valid_ref[0] > 0), s, NEG)
            elif j == nblk - 1:
                s = jnp.where(col <= row, s, NEG)
            else:
                s = jnp.where(valid_ref[j] > 0, s, NEG)
            scores.append(s)
        largest = scores[0].max(axis=1, keepdims=True)
        for s in scores[1:]:
            largest = jnp.maximum(largest, s.max(axis=1, keepdims=True))
        expos = [jnp.exp(s - largest) for s in scores]
        total = expos[0].sum(axis=1, keepdims=True)
        for e in expos[1:]:
            total = total + e.sum(axis=1, keepdims=True)
        inv = 1.0 / total
        out = None
        for j in range(nblk):
            w = (expos[j] * inv).astype(jnp.bfloat16)
            part = jnp.dot(w, v_refs[j][...], preferred_element_type=jnp.float32)
            out = part if out is None else out + part
        o_ref[:, a * HEAD_DIM:(a + 1) * HEAD_DIM] = out.astype(o_ref.dtype)


def attend(valid, queries, k_blocks, v_blocks):
    tok = queries.shape[0]
    group = HEADS // KV_HEADS
    nblk = len(k_blocks)
    kv_spec = pl.BlockSpec((tok, HEAD_DIM), lambda h: (0, h))
    q_spec = pl.BlockSpec((tok, group * HEAD_DIM), lambda h: (0, h))
    flops = 4 * HEADS * tok * tok * nblk * HEAD_DIM
    nbytes = 2 * (2 * queries.size + 2 * nblk * k_blocks[0].size)
    return pl.pallas_call(
        attend_kernel,
        grid=(KV_HEADS,),
        in_specs=[pl.BlockSpec(memory_space=pltpu.SMEM), q_spec]
        + [kv_spec] * (2 * nblk),
        out_specs=q_spec,
        out_shape=jax.ShapeDtypeStruct(queries.shape, queries.dtype),
        cost_estimate=pl.CostEstimate(
            flops=flops, transcendentals=HEADS * tok * tok * nblk, bytes_accessed=nbytes
        ),
    )(valid, queries, *k_blocks, *v_blocks)


def shifted(x, axis, pairs):
    return lax.ppermute(x, axis, pairs)


def body(queries, keys, values):
    axis = ("blk", "grp")
    n = lax.axis_size(axis)
    block_index = lax.axis_index(axis)
    own = (keys, values)
    plane = 2 * lax.axis_size("grp")

    def crossing(t):
        return t % plane < 2

    ahead2 = [(i, i + 2) for i in range(n) if i + 2 < n]
    x1 = shifted(own, axis, ahead2)
    y1 = shifted(own, axis, [(i, i + 1) for i in range(0, n, 2)])
    far = shifted(own, axis, [(i, i + 4) for i in range(n) if i + 4 < n and crossing(i + 4)])
    x2 = shifted(x1, axis, [(i, i + 2) for i in range(n) if i + 2 < n and not crossing(i + 2)])
    first_two = (block_index % plane) < 2
    b4 = [jnp.where(first_two, a, b) for a, b in zip(far, x2)]
    x1_fenced = tuple(lax.optimization_barrier((a, b))[0] for a, b in zip(x1, y1))
    y2 = shifted(x1_fenced, axis, [(i, i ^ 1) for i in range(n)])
    y3 = shifted(b4, axis, [(i, i - 1) for i in range(1, n, 2)])
    odd = (block_index % 2) == 1
    b1 = [jnp.where(odd, a, b) for a, b in zip(y1, y2)]
    b3 = [jnp.where(odd, a, b) for a, b in zip(y2, y3)]
    back_blocks = WINDOW // queries.shape[0]
    nblk = back_blocks + 1
    valid = (block_index + jnp.arange(nblk, dtype=jnp.int32) >= back_blocks).astype(jnp.int32)
    k_blocks = [b4[0], b3[0], x1[0], b1[0], keys]
    v_blocks = [b4[1], b3[1], x1[1], b1[1], values]
    return attend(valid, queries, k_blocks, v_blocks)


def solution(mesh):
    placed = (P(("blk", "grp"), None), P(("blk", "grp"), None), P(("blk", "grp"), None))
    return jax.shard_map(
        body, mesh=mesh, in_specs=placed, out_specs=P(("blk", "grp"), None), check_vma=False
    )
```
